512 devices in a mesh: grp: 16 (over x, z_lo), ep: 32 (over y, z_hi, core).
Axes of the slice: x: 4, y: 8, z: 8 (z_hi: 2, z_lo: 4; z = z_hi * 4 + z_lo), core: 2. Of those that a mesh axis runs over, the one named last changes fastest.
Arguments:
- slot_hidden: bfloat16 [65536, 8, 768], P(('grp', 'ep')), may hold values from -6 to 6
- expert_ids: int32 [65536, 8], P(('grp', 'ep')), may hold values from 0 to 63, all different within a row; in each aligned block of 128 rows (0 to 127, 128 to 255, ...) at most 24 rows name the same one
- gate_fixed: int32 [65536, 8], P(('grp', 'ep')), may hold values from 1 to 65535
- master: float32 [64, 768, 2048], P('ep', 'grp'), may hold values from -6 to 6
- moment_one: bfloat16 [64, 768, 2048], P('ep', 'grp'), may hold values from -3 to 3
- moment_two: bfloat16 [64, 768, 2048], P('ep', 'grp'), may hold values from 0.0099487305 to 2
- gradient: bfloat16 [64, 768, 2048], P('ep', 'grp'), may hold values from -6 to 6
Outputs:
- mixed: bfloat16 [65536, 2048], P(('grp', 'ep'))
- backup: float32 [64, 768, 2048], P('ep', 'grp')
The draws below stay inside these ranges and needn't reach their ends.
Inputs may be any that keep to these rules, and one draw needn't show every extreme that they name: `expert_ids`: in each aligned block of 128 rows (the rows of one device) no expert is named by more than 24 rows, a bound that some block reaches; the 8 experts of a row differ.
All inputs are finite; a program needn't handle non-finite values.
Results may differ from the reference program's by a relative error of at most 0.0057.
Values may be sent and summed in bfloat16 or wider, within the bound.
No kernel may reach another device: no remote copies, remote signals or barrier semaphores. Data moves between devices by JAX's collectives and lax.ppermute only.
A program may use at most 64 MiB of HBM per device.

```python
import math
import jax
import jax.numpy as jnp
import numpy as np
from jax import lax

D = 2048
HID = 768
TOP = 8
TOK_DEV = 128
EXPERTS = 64
CAP = 24
TOKENS = 65536


def set_ends(drawn, rng, low, high):
    dims = drawn.shape
    place = [jax.random.randint(jax.random.fold_in(rng, axis), (), 0, dims[axis]) for axis in range(len(dims))]
    drawn = drawn.at[tuple(place)].set(low)
    longest = dims.index(max(dims))
    place[longest] = (place[longest] + 1) % dims[longest]
    return drawn.at[tuple(place)].set(high)


def levels(rng, shape, cuts, low, top_value):
    level, own = 1.0, jax.random.fold_in(rng, 6)
    for position, parts in cuts:
        steps = jnp.exp(jax.random.uniform(jax.random.fold_in(own, position), (parts,), jnp.float32, low / len(cuts), top_value / len(cuts)))
        level = level * jnp.repeat(steps, shape[position] // parts).reshape([-1 if axis == position else 1 for axis in range(len(shape))])
    return level


def shared_out(rng, own, number, rows, count, top, bound, slope):
    order = jax.random.permutation(rng, count)
    packed, ordinary = shares(count, rows * top, bound, slope, True), shares(count, rows * top, bound, slope, False)
    places = jnp.arange(count)

    def named(tallies, offset_by):
        used = int((tallies > 0).sum())
        fixed = max(1, used // 4)
        shifted = fixed + (places - fixed + offset_by * (used - fixed)) % max(1, count - fixed)
        return jnp.zeros((count,), jnp.int32).at[order[jnp.where(places < fixed, places, shifted)]].set(jnp.asarray(tallies, jnp.int32))

    tallies = jnp.where(number % 4 == 0, named(packed, number // 4), named(ordinary, number - number // 4 - 1))
    mixed = jax.random.permutation(jax.random.fold_in(own, 3), count)
    giver, taker = mixed[0:count // 2 * 2:2], mixed[1:count // 2 * 2:2]
    margin = jnp.minimum(tallies[giver] - 1, bound - tallies[taker]) // 2
    margin = jnp.where((giver == order[0]) | (taker == order[0]) | (tallies[taker] == 0), 0, jnp.maximum(margin, 0))
    shifted = jax.random.randint(jax.random.fold_in(own, 4), (count // 2,), 0, 1 << 20) % (margin + 1)
    tallies = tallies.at[giver].add(-shifted).at[taker].add(shifted)
    items = jnp.searchsorted(jnp.cumsum(tallies), jnp.arange(rows * top), side="right").astype(jnp.int32)
    grid = items.reshape(top, rows).T
    grid = grid[jax.random.permutation(jax.random.fold_in(own, 1), rows)]
    offset_by = jax.random.randint(jax.random.fold_in(own, 2), (rows, 1), 0, top)
    return jnp.take_along_axis(grid, (jnp.arange(top)[None, :] + offset_by) % top, axis=1)


def shares(number_of, total, bound, skew, full):
    loads = [(1 << 20) // math.isqrt(grade ** skew) + 1 for grade in range(1, number_of + 1)]
    largest = bound if full else min(bound, max(-(-total // number_of), total * loads[0] // sum(loads)))
    least = 1 if total - largest >= number_of - 1 else 0
    counts, rest = [largest] + [least] * (number_of - 1), total - largest - least * (number_of - 1)
    while rest > 0:
        candidates = [i for i in range(1, number_of) if counts[i] < largest] or [i for i in range(1, number_of) if counts[i] < bound]
        pool, budget = sum([loads[i] for i in candidates]), rest
        for i in candidates:
            addition = min(bound - counts[i], max(1, budget * loads[i] // pool), rest)
            counts[i] = counts[i] + addition
            rest = rest - addition
    return np.array(counts)


def centred(key, dims, scale, limit, shards=(), kind=jnp.bfloat16):
    factor_of = levels(key, dims, shards, -0.22, 0.18) if shards else 1.0
    values = jax.random.normal(key, dims, jnp.float32) * scale * factor_of
    return jnp.minimum(jnp.maximum(values, -limit), limit).astype(kind)


def setup_inputs(seed: int = 0) -> dict:
    keys = jax.random.split(jax.random.key(seed), 8)
    slot_hidden = centred(keys[0], (TOKENS, TOP, HID), 1.0, 6.0, ((0, 512),))
    expert_ids_keys = jax.random.split(jax.random.fold_in(keys[1], 1), TOKENS // TOK_DEV)
    expert_ids_turns = jax.random.permutation(jax.random.fold_in(keys[1], 3), TOKENS // TOK_DEV)
    expert_ids = jax.vmap(lambda own, number: shared_out(jax.random.fold_in(keys[1], 2), own, number, TOK_DEV, EXPERTS, TOP, CAP, 1))(expert_ids_keys, expert_ids_turns).reshape((TOKENS, TOP))
    gate_fixed = set_ends(jax.random.randint(keys[2], (TOKENS, TOP), 1, 65536), jax.random.fold_in(keys[2], 1), 1, 65535).astype(jnp.int32)
    master = centred(keys[3], (EXPERTS, HID, D), 1.0, 6.0, ((0, 32), (1, 16)), jnp.float32)
    moment_one = centred(keys[4], (EXPERTS, HID, D), 0.5, 3.0, ((0, 32), (1, 16)))
    moment_two = jnp.clip(jnp.exp(math.log(2.0) - 5.3034575 * jax.random.uniform(keys[5], (EXPERTS, HID, D), jnp.float32) ** levels(keys[5], (EXPERTS, HID, D), ((0, 32), (1, 16)), -0.2, 0.2)), 0.0099487305, 2.0).astype(jnp.bfloat16)
    gradient = centred(keys[6], (EXPERTS, HID, D), 1.0, 6.0, ((0, 32), (1, 16)))
    return dict(slot_hidden=slot_hidden, expert_ids=expert_ids, gate_fixed=gate_fixed, master=master, moment_one=moment_one, moment_two=moment_two, gradient=gradient)


beta_one = 0.9
beta_two = 0.95
corr_one = 1.0 - 0.9 ** 40
corr_two = 1.0 - 0.95 ** 40
learn_rate = 0.05
decay_rate = 0.1
adam_eps = 1e-08
gate_unit = 65536.0

def adamw_step(master, moment_one, moment_two, gradient):
    widened = gradient.astype(jnp.float32)
    first_moment = beta_one * moment_one.astype(jnp.float32) + (1.0 - beta_one) * widened
    second_moment = beta_two * moment_two.astype(jnp.float32) + (1.0 - beta_two) * widened * widened
    return first_moment / corr_one / (jnp.sqrt(second_moment / corr_two) + adam_eps) + decay_rate * master

def slot_positions(ids_block, experts, capacity):
    onehot = (ids_block[:, None] == jnp.arange(experts, dtype=jnp.int32)[None, :]).astype(jnp.int32)
    before = jnp.cumsum(onehot, axis=0) - onehot
    slot_index = lax.optimization_barrier(jnp.sum(before * onehot, axis=1))
    return (ids_block * capacity + slot_index).astype(jnp.int32)

def partial_slots(row):
    return slot_positions(row, EXPERTS, CAP)

def reference(slot_hidden, expert_ids, gate_fixed, master, moment_one, moment_two, gradient):
    step_dir = adamw_step(master, moment_one, moment_two, gradient)
    updated = master - learn_rate * step_dir
    backup = jnp.roll(step_dir, -(HID // 2), axis=1)
    weights = updated.astype(jnp.bfloat16)
    scaling = 1.0 / math.sqrt(HID)
    blocks = TOKENS // TOK_DEV
    pairs = TOK_DEV * TOP
    sentinel = blocks * pairs
    id_blocks = expert_ids.reshape(blocks, pairs).astype(jnp.int32)
    positions = jax.vmap(partial_slots)(id_blocks)
    rows_global = (jnp.arange(blocks, dtype=jnp.int32)[:, None] * pairs + jnp.arange(pairs, dtype=jnp.int32)[None, :]).astype(jnp.int32)
    table = jnp.full((blocks, EXPERTS * CAP), sentinel, jnp.int32)
    table = table.at[jnp.arange(blocks, dtype=jnp.int32)[:, None], positions].set(rows_global)
    table = table.reshape(blocks, EXPERTS, CAP).transpose(1, 0, 2).reshape(EXPERTS, blocks * CAP)
    hidden_rows = jnp.concatenate([slot_hidden.reshape(sentinel, HID), jnp.zeros((1, HID), jnp.bfloat16)], 0)
    factor_rows = jnp.concatenate([gate_fixed.reshape(sentinel).astype(jnp.float32) / gate_unit, jnp.zeros((1,), jnp.float32)], 0)

    def add_expert(total, inputs):
        index_row, expert_weight = inputs
        picked = hidden_rows[index_row]
        result = (jnp.dot(picked, expert_weight, preferred_element_type=jnp.float32) * scaling).astype(jnp.bfloat16)
        target = (index_row // TOP).astype(jnp.int32)
        total = total.at[target].add(result.astype(jnp.float32) * factor_rows[index_row][:, None])
        return (total, None)
    total, unused = lax.scan(add_expert, jnp.zeros((TOKENS + 1, D), jnp.float32), (table, weights))
    mixed = total[:TOKENS].astype(jnp.bfloat16)
    return (mixed, backup)
```

```python
import math

import jax
import jax.numpy as jnp
from jax import lax
from jax.sharding import PartitionSpec as P

beta_one = 0.9
beta_two = 0.95
corr_one = 1.0 - 0.9**40
corr_two = 1.0 - 0.95**40
learn_rate = 0.05
decay_rate = 0.1
adam_eps = 1e-08
gate_unit = 65536.0


def adamw_step(master, moment_one, moment_two, gradient):
    widened = gradient.astype(jnp.float32)
    first_moment = beta_one * moment_one.astype(jnp.float32) + (1.0 - beta_one) * widened
    second_moment = beta_two * moment_two.astype(jnp.float32) + (1.0 - beta_two) * widened * widened
    return (
        first_moment / corr_one / (jnp.sqrt(second_moment / corr_two) + adam_eps)
        + decay_rate * master
    )


def slot_positions(ids, capacity):
    count = ids.shape[0]
    rows = lax.broadcasted_iota(jnp.int32, (count, count), 0)
    cols = lax.broadcasted_iota(jnp.int32, (count, count), 1)
    same = (ids[:, None] == ids[None, :]) & (cols < rows)
    slot_index = jnp.sum(same.astype(jnp.int32), axis=1)
    return ids * capacity + slot_index


def body(slot_hidden, expert_ids, gate_fixed, master, moment_one, moment_two, gradient):
    groups = lax.axis_size("grp")
    ranks = lax.axis_size("ep")
    local_experts = master.shape[0]
    experts = local_experts * ranks
    tok_count, top_count, hidden_width = slot_hidden.shape
    width = master.shape[2]
    capacity = max(2, tok_count * top_count // experts + tok_count * top_count // (2 * experts))
    slots = experts * capacity
    scaling = 1.0 / math.sqrt(hidden_width)

    step_dir = adamw_step(master, moment_one, moment_two, gradient)
    updated = master - learn_rate * step_dir
    weights = updated.astype(jnp.bfloat16)
    gathered = lax.all_gather(weights, "grp", axis=1, tiled=True)

    shift = groups // 2
    backup = lax.ppermute(step_dir, "grp", [(s, (s + shift) % groups) for s in range(groups)])

    pairs = tok_count * top_count
    positions = slot_positions(expert_ids.reshape(pairs), capacity)
    slot_ids = lax.broadcasted_iota(jnp.int32, (slots, pairs), 0)
    placing = (positions[None, :] == slot_ids).astype(jnp.bfloat16)
    outgoing = jnp.dot(placing, slot_hidden.reshape(pairs, hidden_width),
                       preferred_element_type=jnp.float32).astype(jnp.bfloat16)
    outgoing = outgoing.reshape(experts, capacity, hidden_width)
    arrived = lax.all_to_all(outgoing, "ep", split_axis=0, concat_axis=1, tiled=True)

    product = jnp.einsum("erh,ehd->erd", arrived, gathered, preferred_element_type=jnp.float32)
    results = (product * scaling).astype(jnp.bfloat16)
    tiles = results.reshape(local_experts, ranks, capacity, width).transpose(1, 0, 2, 3)
    returned = lax.all_to_all(tiles, "ep", split_axis=0, concat_axis=0, tiled=True)
    returned = returned.reshape(slots, width)

    factors = gate_fixed.astype(jnp.float32) / gate_unit
    token_pos = positions.reshape(tok_count, top_count)
    slot_row = lax.broadcasted_iota(jnp.int32, (tok_count, top_count, slots), 2)
    combine = jnp.sum(jnp.where(token_pos[:, :, None] == slot_row, factors[:, :, None], 0.0), axis=1)
    combine_hi = combine.astype(jnp.bfloat16)
    combine_lo = (combine - combine_hi.astype(jnp.float32)).astype(jnp.bfloat16)
    mixed = jnp.dot(combine_hi, returned, preferred_element_type=jnp.float32) + jnp.dot(
        combine_lo, returned, preferred_element_type=jnp.float32)
    return (mixed.astype(jnp.bfloat16), backup)


def solution(mesh):
    tokens = P(("grp", "ep"), None, None)
    pair_spec = P(("grp", "ep"), None)
    state = P("ep", "grp", None)
    in_specs = (tokens, pair_spec, pair_spec, state, state, state, state)
    out_specs = (pair_spec, state)
    return jax.shard_map(body, mesh=mesh, in_specs=in_specs, out_specs=out_specs, check_vma=False)
```

```python
import math

import jax
import jax.numpy as jnp
from jax import lax
from jax.sharding import Mesh
from jax.sharding import PartitionSpec as P

GRP = ("grp_0", "grp_1")

beta_one = 0.9
beta_two = 0.95
corr_one = 1.0 - 0.9**40
corr_two = 1.0 - 0.95**40
learn_rate = 0.05
decay_rate = 0.1
adam_eps = 1e-08
gate_unit = 65536.0


def adamw_step(master, moment_one, moment_two, gradient):
    widened = gradient.astype(jnp.float32)
    first_moment = beta_one * moment_one.astype(jnp.float32) + (1.0 - beta_one) * widened
    second_moment = beta_two * moment_two.astype(jnp.float32) + (1.0 - beta_two) * widened * widened
    return (
        first_moment / corr_one / (jnp.sqrt(second_moment / corr_two) + adam_eps)
        + decay_rate * master
    )


def slot_positions(ids, capacity):
    count = ids.shape[0]
    rows = lax.broadcasted_iota(jnp.int32, (count, count), 0)
    cols = lax.broadcasted_iota(jnp.int32, (count, count), 1)
    same = (ids[:, None] == ids[None, :]) & (cols < rows)
    slot_index = jnp.sum(same.astype(jnp.int32), axis=1)
    return ids * capacity + slot_index


def body(slot_hidden, expert_ids, gate_fixed, master, moment_one, moment_two, gradient):
    outer = lax.axis_size("grp_0")
    ranks = lax.axis_size("ep")
    local_experts = master.shape[0]
    experts = local_experts * ranks
    tok_count, top_count, hidden_width = slot_hidden.shape
    width = master.shape[2]
    capacity = max(2, tok_count * top_count // experts + tok_count * top_count // (2 * experts))
    slots = experts * capacity
    scaling = 1.0 / math.sqrt(hidden_width)

    step_dir = adamw_step(master, moment_one, moment_two, gradient)
    updated = master - learn_rate * step_dir
    weights = updated.astype(jnp.bfloat16)
    nearer = lax.all_gather(weights, "grp_1", axis=1, tiled=True)
    gathered = lax.all_gather(nearer, "grp_0", axis=1, tiled=True)

    shift = outer // 2
    backup = lax.ppermute(step_dir, "grp_0", [(s, (s + shift) % outer) for s in range(outer)])

    pairs = tok_count * top_count
    positions = slot_positions(expert_ids.reshape(pairs), capacity)
    slot_ids = lax.broadcasted_iota(jnp.int32, (slots, pairs), 0)
    placing = (positions[None, :] == slot_ids).astype(jnp.bfloat16)
    outgoing = jnp.dot(placing, slot_hidden.reshape(pairs, hidden_width),
                       preferred_element_type=jnp.float32).astype(jnp.bfloat16)
    outgoing = outgoing.reshape(experts, capacity, hidden_width)
    arrived = lax.all_to_all(outgoing, "ep", split_axis=0, concat_axis=1, tiled=True)

    product = jnp.einsum("erh,ehd->erd", arrived, gathered, preferred_element_type=jnp.float32)
    results = (product * scaling).astype(jnp.bfloat16)
    tiles = results.reshape(local_experts, ranks, capacity, width).transpose(1, 0, 2, 3)

    high = (gate_fixed // 256).astype(jnp.float32) / 256.0
    low = (gate_fixed % 256).astype(jnp.float32) / gate_unit
    token_pos = positions.reshape(tok_count, top_count)
    slot_row = lax.broadcasted_iota(jnp.int32, (tok_count, top_count, slots), 2)
    hit = token_pos[:, :, None] == slot_row
    combine_hi = jnp.sum(jnp.where(hit, high[:, :, None], 0.0), axis=1).astype(jnp.bfloat16)
    combine_lo = jnp.sum(jnp.where(hit, low[:, :, None], 0.0), axis=1).astype(jnp.bfloat16)
    combine_hi = combine_hi.reshape(tok_count, experts, capacity)
    combine_lo = combine_lo.reshape(tok_count, experts, capacity)

    mixed = jnp.zeros((tok_count, width), jnp.float32)
    half = capacity // 2
    for start, stop in ((0, half), (half, capacity)):
        piece = lax.all_to_all(tiles[:, :, start:stop], "ep", split_axis=0, concat_axis=0, tiled=True)
        piece = piece.reshape(experts * (stop - start), width)
        for part in (combine_hi, combine_lo):
            weight = part[:, :, start:stop].reshape(tok_count, experts * (stop - start))
            mixed = mixed + jnp.dot(weight, piece, preferred_element_type=jnp.float32)
    return (mixed.astype(jnp.bfloat16), backup)


def solution(mesh):
    torus = Mesh(mesh.devices.reshape(4, 4, mesh.shape["ep"]), ("grp_0", "grp_1", "ep"))
    tokens = P(GRP + ("ep",), None, None)
    pair_spec = P(GRP + ("ep",), None)
    state = P("ep", GRP, None)
    in_specs = (tokens, pair_spec, pair_spec, state, state, state, state)
    out_specs = (pair_spec, state)
    return jax.shard_map(body, mesh=torus, in_specs=in_specs, out_specs=out_specs, check_vma=False)
```

```python
import math

import jax
import jax.numpy as jnp
from jax import lax
from jax.sharding import Mesh
from jax.sharding import PartitionSpec as P

GRP = ("grp_0", "grp_1")

beta_one = 0.9
beta_two = 0.95
corr_one = 1.0 - 0.9**40
corr_two = 1.0 - 0.95**40
learn_rate = 0.05
decay_rate = 0.1
adam_eps = 1e-08
gate_unit = 65536.0


def adamw_step(master, moment_one, moment_two, gradient):
    widened = gradient.astype(jnp.float32)
    first_moment = beta_one * moment_one.astype(jnp.float32) + (1.0 - beta_one) * widened
    second_moment = beta_two * moment_two.astype(jnp.float32) + (1.0 - beta_two) * widened * widened
    return (
        first_moment / corr_one / (jnp.sqrt(second_moment / corr_two) + adam_eps)
        + decay_rate * master
    )


def slot_positions(ids, capacity):
    count = ids.shape[0]
    rows = lax.broadcasted_iota(jnp.int32, (count, count), 0)
    cols = lax.broadcasted_iota(jnp.int32, (count, count), 1)
    same = (ids[:, None] == ids[None, :]) & (cols < rows)
    slot_index = jnp.sum(same.astype(jnp.int32), axis=1)
    return ids * capacity + slot_index


def body(slot_hidden, expert_ids, gate_fixed, master, moment_one, moment_two, gradient):
    outer = lax.axis_size("grp_0")
    ranks = lax.axis_size("ep")
    local_experts = master.shape[0]
    experts = local_experts * ranks
    tok_count, top_count, hidden_width = slot_hidden.shape
    width = master.shape[2]
    capacity = max(2, tok_count * top_count // experts + tok_count * top_count // (2 * experts))
    slots = experts * capacity
    scaling = 1.0 / math.sqrt(hidden_width)

    step_dir = adamw_step(master, moment_one, moment_two, gradient)
    updated = master - learn_rate * step_dir
    weights = updated.astype(jnp.bfloat16)
    nearer = lax.all_gather(weights, "grp_1", axis=1, tiled=True)
    gathered = lax.all_gather(nearer, "grp_0", axis=1, tiled=True)

    shift = outer // 2
    backup = lax.ppermute(step_dir, "grp_0", [(s, (s + shift) % outer) for s in range(outer)])

    pairs = tok_count * top_count
    positions = slot_positions(expert_ids.reshape(pairs), capacity)
    hidden_rows = slot_hidden.reshape(pairs, hidden_width)
    token_pos = positions.reshape(tok_count, top_count)
    high = (gate_fixed // 256).astype(jnp.float32) / 256.0
    low = (gate_fixed % 256).astype(jnp.float32) / gate_unit
    chunk = ranks * capacity

    mixed = jnp.zeros((tok_count, width), jnp.float32)
    for local in range(local_experts):
        column = lax.broadcasted_iota(jnp.int32, (chunk,), 0)
        slot_of = ((column // capacity) * local_experts + local) * capacity + column % capacity
        placing = (positions[None, :] == slot_of[:, None]).astype(jnp.bfloat16)
        outgoing = jnp.dot(placing, hidden_rows, preferred_element_type=jnp.float32).astype(jnp.bfloat16)
        arrived = lax.all_to_all(outgoing.reshape(ranks, capacity, hidden_width), "ep",
                                 split_axis=0, concat_axis=0, tiled=True)
        product = jnp.dot(arrived.reshape(chunk, hidden_width), gathered[local],
                          preferred_element_type=jnp.float32)
        results = (product * scaling).astype(jnp.bfloat16)
        returned = lax.all_to_all(results.reshape(ranks, capacity, width), "ep",
                                  split_axis=0, concat_axis=0, tiled=True)
        returned = returned.reshape(chunk, width)
        hit = token_pos[:, :, None] == slot_of[None, None, :]
        for part in (high, low):
            weight = jnp.sum(jnp.where(hit, part[:, :, None], 0.0), axis=1).astype(jnp.bfloat16)
            mixed = mixed + jnp.dot(weight, returned, preferred_element_type=jnp.float32)
    return (mixed.astype(jnp.bfloat16), backup)


def solution(mesh):
    torus = Mesh(mesh.devices.reshape(4, 4, mesh.shape["ep"]), ("grp_0", "grp_1", "ep"))
    tokens = P(GRP + ("ep",), None, None)
    pair_spec = P(GRP + ("ep",), None)
    state = P("ep", GRP, None)
    in_specs = (tokens, pair_spec, pair_spec, state, state, state, state)
    out_specs = (pair_spec, state)
    return jax.shard_map(body, mesh=torus, in_specs=in_specs, out_specs=out_specs, check_vma=False)
```

```python
import math

import jax
import jax.numpy as jnp
from jax import lax
from jax.sharding import Mesh
from jax.sharding import PartitionSpec as P

GRP = ("grp_0", "grp_1")

beta_one = 0.9
beta_two = 0.95
corr_one = 1.0 - 0.9**40
corr_two = 1.0 - 0.95**40
learn_rate = 0.05
decay_rate = 0.1
adam_eps = 1e-08
gate_unit = 65536.0


def adamw_step(master, moment_one, moment_two, gradient):
    widened = gradient.astype(jnp.float32)
    first_moment = beta_one * moment_one.astype(jnp.float32) + (1.0 - beta_one) * widened
    second_moment = beta_two * moment_two.astype(jnp.float32) + (1.0 - beta_two) * widened * widened
    return (
        first_moment / corr_one / (jnp.sqrt(second_moment / corr_two) + adam_eps)
        + decay_rate * master
    )


def slot_positions(ids, capacity):
    count = ids.shape[0]
    rows = lax.broadcasted_iota(jnp.int32, (count, count), 0)
    cols = lax.broadcasted_iota(jnp.int32, (count, count), 1)
    same = (ids[:, None] == ids[None, :]) & (cols < rows)
    slot_index = jnp.sum(same.astype(jnp.int32), axis=1)
    return ids * capacity + slot_index


def body(slot_hidden, expert_ids, gate_fixed, master, moment_one, moment_two, gradient):
    outer = lax.axis_size("grp_0")
    ranks = lax.axis_size("ep")
    local_experts = master.shape[0]
    experts = local_experts * ranks
    tok_count, top_count, hidden_width = slot_hidden.shape
    width = master.shape[2]
    capacity = max(2, tok_count * top_count // experts + tok_count * top_count // (2 * experts))
    slots = experts * capacity
    scaling = 1.0 / math.sqrt(hidden_width)

    step_dir = adamw_step(master, moment_one, moment_two, gradient)
    updated = master - learn_rate * step_dir
    weights = updated.astype(jnp.bfloat16)
    nearer = lax.all_gather(weights, "grp_1", axis=1, tiled=True)
    gathered = []
    for local in range(local_experts):
        rows = nearer[local]
        if gathered:
            rows, _ = lax.optimization_barrier((rows, gathered[-1]))
        gathered.append(lax.all_gather(rows, "grp_0", axis=0, tiled=True))

    shift = outer // 2
    backup = lax.ppermute(step_dir, "grp_0", [(s, (s + shift) % outer) for s in range(outer)])

    pairs = tok_count * top_count
    positions = slot_positions(expert_ids.reshape(pairs), capacity)
    hidden_rows = slot_hidden.reshape(pairs, hidden_width)
    token_pos = positions.reshape(tok_count, top_count)
    high = (gate_fixed // 256).astype(jnp.float32) / 256.0
    low = (gate_fixed % 256).astype(jnp.float32) / gate_unit
    chunk = ranks * capacity

    mixed = jnp.zeros((tok_count, width), jnp.float32)
    for local in range(local_experts):
        column = lax.broadcasted_iota(jnp.int32, (chunk,), 0)
        slot_of = ((column // capacity) * local_experts + local) * capacity + column % capacity
        placing = (positions[None, :] == slot_of[:, None]).astype(jnp.bfloat16)
        outgoing = jnp.dot(placing, hidden_rows, preferred_element_type=jnp.float32).astype(jnp.bfloat16)
        arrived = lax.all_to_all(outgoing.reshape(ranks, capacity, hidden_width), "ep",
                                 split_axis=0, concat_axis=0, tiled=True)
        product = jnp.dot(arrived.reshape(chunk, hidden_width), gathered[local],
                          preferred_element_type=jnp.float32)
        results = (product * scaling).astype(jnp.bfloat16)
        returned = lax.all_to_all(results.reshape(ranks, capacity, width), "ep",
                                  split_axis=0, concat_axis=0, tiled=True)
        returned = returned.reshape(chunk, width)
        hit = token_pos[:, :, None] == slot_of[None, None, :]
        for part in (high, low):
            weight = jnp.sum(jnp.where(hit, part[:, :, None], 0.0), axis=1).astype(jnp.bfloat16)
            mixed = mixed + jnp.dot(weight, returned, preferred_element_type=jnp.float32)
    return (mixed.astype(jnp.bfloat16), backup)


def solution(mesh):
    torus = Mesh(mesh.devices.reshape(4, 4, mesh.shape["ep"]), ("grp_0", "grp_1", "ep"))
    tokens = P(GRP + ("ep",), None, None)
    pair_spec = P(GRP + ("ep",), None)
    state = P("ep", GRP, None)
    in_specs = (tokens, pair_spec, pair_spec, state, state, state, state)
    out_specs = (pair_spec, state)
    return jax.shard_map(body, mesh=torus, in_specs=in_specs, out_specs=out_specs, check_vma=False)
```

```python
import math

import jax
import jax.numpy as jnp
from jax import lax
from jax.sharding import Mesh
from jax.sharding import PartitionSpec as P

GRP = ("grp_0", "grp_1")

beta_one = 0.9
beta_two = 0.95
corr_one = 1.0 - 0.9**40
corr_two = 1.0 - 0.95**40
learn_rate = 0.05
decay_rate = 0.1
adam_eps = 1e-08
gate_unit = 65536.0


def adamw_step(master, moment_one, moment_two, gradient):
    widened = gradient.astype(jnp.float32)
    first_moment = beta_one * moment_one.astype(jnp.float32) + (1.0 - beta_one) * widened
    second_moment = beta_two * moment_two.astype(jnp.float32) + (1.0 - beta_two) * widened * widened
    return (
        first_moment / corr_one / (jnp.sqrt(second_moment / corr_two) + adam_eps)
        + decay_rate * master
    )


def slot_positions(ids, capacity):
    count = ids.shape[0]
    rows = lax.broadcasted_iota(jnp.int32, (count, count), 0)
    cols = lax.broadcasted_iota(jnp.int32, (count, count), 1)
    same = (ids[:, None] == ids[None, :]) & (cols < rows)
    slot_index = jnp.sum(same.astype(jnp.int32), axis=1)
    return ids * capacity + slot_index


def body(slot_hidden, expert_ids, gate_fixed, master, moment_one, moment_two, gradient):
    outer = lax.axis_size("grp_0")
    ranks = lax.axis_size("ep")
    local_experts = master.shape[0]
    experts = local_experts * ranks
    tok_count, top_count, hidden_width = slot_hidden.shape
    width = master.shape[2]
    capacity = max(2, tok_count * top_count // experts + tok_count * top_count // (2 * experts))
    slots = experts * capacity
    scaling = 1.0 / math.sqrt(hidden_width)

    step_dir = adamw_step(master, moment_one, moment_two, gradient)
    updated = master - learn_rate * step_dir
    weights = updated.astype(jnp.bfloat16)
    inner = lax.axis_size("grp_1")
    here = lax.axis_index("grp_1")
    received = [weights]
    for shift_by in range(1, inner):
        received.append(lax.ppermute(weights, "grp_1", [(s, (s + shift_by) % inner) for s in range(inner)]))
    ordered = jnp.stack([received[(-k) % inner] for k in range(inner)], axis=1)
    ordered = jnp.roll(ordered, here, axis=1)
    nearer = ordered.reshape(local_experts, inner * weights.shape[1], width)
    gathered = []
    for local in range(local_experts):
        rows = nearer[local]
        if gathered:
            rows, _ = lax.optimization_barrier((rows, gathered[-1]))
        gathered.append(lax.all_gather(rows, "grp_0", axis=0, tiled=True))

    shift = outer // 2
    backup = lax.ppermute(step_dir, "grp_0", [(s, (s + shift) % outer) for s in range(outer)])

    pairs = tok_count * top_count
    positions = slot_positions(expert_ids.reshape(pairs), capacity)
    hidden_rows = slot_hidden.reshape(pairs, hidden_width)
    token_pos = positions.reshape(tok_count, top_count)
    high = (gate_fixed // 256).astype(jnp.float32) / 256.0
    low = (gate_fixed % 256).astype(jnp.float32) / gate_unit
    chunk = ranks * capacity

    mixed = jnp.zeros((tok_count, width), jnp.float32)
    for local in range(local_experts):
        column = lax.broadcasted_iota(jnp.int32, (chunk,), 0)
        slot_of = ((column // capacity) * local_experts + local) * capacity + column % capacity
        placing = (positions[None, :] == slot_of[:, None]).astype(jnp.bfloat16)
        outgoing = jnp.dot(placing, hidden_rows, preferred_element_type=jnp.float32).astype(jnp.bfloat16)
        arrived = lax.all_to_all(outgoing.reshape(ranks, capacity, hidden_width), "ep",
                                 split_axis=0, concat_axis=0, tiled=True)
        product = jnp.dot(arrived.reshape(chunk, hidden_width), gathered[local],
                          preferred_element_type=jnp.float32)
        results = (product * scaling).astype(jnp.bfloat16)
        returned = lax.all_to_all(results.reshape(ranks, capacity, width), "ep",
                                  split_axis=0, concat_axis=0, tiled=True)
        returned = returned.reshape(chunk, width)
        hit = token_pos[:, :, None] == slot_of[None, None, :]
        for part in (high, low):
            weight = jnp.sum(jnp.where(hit, part[:, :, None], 0.0), axis=1).astype(jnp.bfloat16)
            mixed = mixed + jnp.dot(weight, returned, preferred_element_type=jnp.float32)
    return (mixed.astype(jnp.bfloat16), backup)


def solution(mesh):
    torus = Mesh(mesh.devices.reshape(4, 4, mesh.shape["ep"]), ("grp_0", "grp_1", "ep"))
    tokens = P(GRP + ("ep",), None, None)
    pair_spec = P(GRP + ("ep",), None)
    state = P("ep", GRP, None)
    in_specs = (tokens, pair_spec, pair_spec, state, state, state, state)
    out_specs = (pair_spec, state)
    return jax.shard_map(body, mesh=torus, in_specs=in_specs, out_specs=out_specs, check_vma=False)
```

```python
import math

import jax
import jax.numpy as jnp
from jax import lax
from jax.sharding import Mesh
from jax.sharding import PartitionSpec as P

GRP = ("grp_0", "grp_1")

beta_one = 0.9
beta_two = 0.95
corr_one = 1.0 - 0.9**40
corr_two = 1.0 - 0.95**40
learn_rate = 0.05
decay_rate = 0.1
adam_eps = 1e-08
gate_unit = 65536.0


def adamw_step(master, moment_one, moment_two, gradient):
    widened = gradient.astype(jnp.float32)
    first_moment = beta_one * moment_one.astype(jnp.float32) + (1.0 - beta_one) * widened
    second_moment = beta_two * moment_two.astype(jnp.float32) + (1.0 - beta_two) * widened * widened
    return (
        first_moment / corr_one / (jnp.sqrt(second_moment / corr_two) + adam_eps)
        + decay_rate * master
    )


def slot_positions(ids, capacity):
    count = ids.shape[0]
    rows = lax.broadcasted_iota(jnp.int32, (count, count), 0)
    cols = lax.broadcasted_iota(jnp.int32, (count, count), 1)
    same = (ids[:, None] == ids[None, :]) & (cols < rows)
    slot_index = jnp.sum(same.astype(jnp.int32), axis=1)
    return ids * capacity + slot_index


def body(slot_hidden, expert_ids, gate_fixed, master, moment_one, moment_two, gradient):
    outer = lax.axis_size("grp_0")
    ranks = lax.axis_size("ep")
    local_experts = master.shape[0]
    experts = local_experts * ranks
    tok_count, top_count, hidden_width = slot_hidden.shape
    width = master.shape[2]
    capacity = max(2, tok_count * top_count // experts + tok_count * top_count // (2 * experts))
    slots = experts * capacity
    scaling = 1.0 / math.sqrt(hidden_width)

    step_dir = adamw_step(master, moment_one, moment_two, gradient)
    updated = master - learn_rate * step_dir
    weights = updated.astype(jnp.bfloat16)
    nearer = lax.all_gather(weights, "grp_1", axis=1, tiled=True)

    shift = outer // 2
    backup = lax.ppermute(step_dir, "grp_0", [(s, (s + shift) % outer) for s in range(outer)])

    pairs = tok_count * top_count
    positions = slot_positions(expert_ids.reshape(pairs), capacity)
    hidden_rows = slot_hidden.reshape(pairs, hidden_width)
    token_pos = positions.reshape(tok_count, top_count)
    high = (gate_fixed // 256).astype(jnp.float32) / 256.0
    low = (gate_fixed % 256).astype(jnp.float32) / gate_unit
    chunk = ranks * capacity

    column = lax.broadcasted_iota(jnp.int32, (chunk,), 0)
    slot_of = []
    arrived = []
    for local in range(local_experts):
        slot_of.append(((column // capacity) * local_experts + local) * capacity + column % capacity)
        placing = (positions[None, :] == slot_of[local][:, None]).astype(jnp.bfloat16)
        outgoing = jnp.dot(placing, hidden_rows, preferred_element_type=jnp.float32).astype(jnp.bfloat16)
        arrived.append(lax.all_to_all(outgoing.reshape(ranks, capacity, hidden_width), "ep",
                                      split_axis=0, concat_axis=0, tiled=True))

    gathered = []
    for local in range(local_experts):
        rows, tie = lax.optimization_barrier((nearer[local], gathered[-1] if gathered else arrived[0]))
        if not gathered:
            arrived[0] = tie
        gathered.append(lax.all_gather(rows, "grp_0", axis=0, tiled=True))

    mixed = jnp.zeros((tok_count, width), jnp.float32)
    for local in range(local_experts):
        product = jnp.dot(arrived[local].reshape(chunk, hidden_width), gathered[local],
                          preferred_element_type=jnp.float32)
        results = (product * scaling).astype(jnp.bfloat16)
        returned = lax.all_to_all(results.reshape(ranks, capacity, width), "ep",
                                  split_axis=0, concat_axis=0, tiled=True)
        returned = returned.reshape(chunk, width)
        hit = token_pos[:, :, None] == slot_of[local][None, None, :]
        for part in (high, low):
            weight = jnp.sum(jnp.where(hit, part[:, :, None], 0.0), axis=1).astype(jnp.bfloat16)
            mixed = mixed + jnp.dot(weight, returned, preferred_element_type=jnp.float32)
    return (mixed.astype(jnp.bfloat16), backup)


def solution(mesh):
    torus = Mesh(mesh.devices.reshape(4, 4, mesh.shape["ep"]), ("grp_0", "grp_1", "ep"))
    tokens = P(GRP + ("ep",), None, None)
    pair_spec = P(GRP + ("ep",), None)
    state = P("ep", GRP, None)
    in_specs = (tokens, pair_spec, pair_spec, state, state, state, state)
    out_specs = (pair_spec, state)
    return jax.shard_map(body, mesh=torus, in_specs=in_specs, out_specs=out_specs, check_vma=False)
```

```python
import math

import jax
import jax.numpy as jnp
from jax import lax
from jax.sharding import Mesh
from jax.sharding import PartitionSpec as P

GRP = ("grp_0", "grp_1")

beta_one = 0.9
beta_two = 0.95
corr_one = 1.0 - 0.9**40
corr_two = 1.0 - 0.95**40
learn_rate = 0.05
decay_rate = 0.1
adam_eps = 1e-08
gate_unit = 65536.0


def adamw_step(master, moment_one, moment_two, gradient):
    widened = gradient.astype(jnp.float32)
    first_moment = beta_one * moment_one.astype(jnp.float32) + (1.0 - beta_one) * widened
    second_moment = beta_two * moment_two.astype(jnp.float32) + (1.0 - beta_two) * widened * widened
    return (
        first_moment / corr_one / (jnp.sqrt(second_moment / corr_two) + adam_eps)
        + decay_rate * master
    )


def slot_positions(ids, capacity):
    count = ids.shape[0]
    rows = lax.broadcasted_iota(jnp.int32, (count, count), 0)
    cols = lax.broadcasted_iota(jnp.int32, (count, count), 1)
    same = (ids[:, None] == ids[None, :]) & (cols < rows)
    slot_index = jnp.sum(same.astype(jnp.int32), axis=1)
    return ids * capacity + slot_index


def body(slot_hidden, expert_ids, gate_fixed, master, moment_one, moment_two, gradient):
    outer = lax.axis_size("grp_0")
    ranks = lax.axis_size("ep")
    local_experts = master.shape[0]
    experts = local_experts * ranks
    tok_count, top_count, hidden_width = slot_hidden.shape
    width = master.shape[2]
    capacity = max(2, tok_count * top_count // experts + tok_count * top_count // (2 * experts))
    slots = experts * capacity
    scaling = 1.0 / math.sqrt(hidden_width)

    step_dir = adamw_step(master, moment_one, moment_two, gradient)
    updated = master - learn_rate * step_dir
    weights = updated.astype(jnp.bfloat16)
    inner = lax.axis_size("grp_1")
    nearer = lax.all_gather(weights, "grp_0", axis=1, tiled=True)

    shift = outer // 2
    backup = lax.ppermute(step_dir, "grp_0", [(s, (s + shift) % outer) for s in range(outer)])

    pairs = tok_count * top_count
    positions = slot_positions(expert_ids.reshape(pairs), capacity)
    hidden_rows = slot_hidden.reshape(pairs, hidden_width)
    token_pos = positions.reshape(tok_count, top_count)
    high = (gate_fixed // 256).astype(jnp.float32) / 256.0
    low = (gate_fixed % 256).astype(jnp.float32) / gate_unit
    chunk = ranks * capacity

    column = lax.broadcasted_iota(jnp.int32, (chunk,), 0)
    slot_of = []
    arrived = []
    for local in range(local_experts):
        slot_of.append(((column // capacity) * local_experts + local) * capacity + column % capacity)
        placing = (positions[None, :] == slot_of[local][:, None]).astype(jnp.bfloat16)
        outgoing = jnp.dot(placing, hidden_rows, preferred_element_type=jnp.float32).astype(jnp.bfloat16)
        arrived.append(lax.all_to_all(outgoing.reshape(ranks, capacity, hidden_width), "ep",
                                      split_axis=0, concat_axis=0, tiled=True))

    gathered = []
    for local in range(local_experts):
        rows, tie = lax.optimization_barrier((nearer[local], gathered[-1] if gathered else arrived[0]))
        if not gathered:
            arrived[0] = tie
        gathered.append(lax.all_gather(rows, "grp_1", axis=0, tiled=True))

    mixed = jnp.zeros((tok_count, width), jnp.float32)
    for local in range(local_experts):
        block = weights.shape[1]
        product = jnp.einsum(
            "cxzh,zxhd->cd", arrived[local].reshape(chunk, outer, inner, block),
            gathered[local].reshape(inner, outer, block, width), preferred_element_type=jnp.float32)
        results = (product * scaling).astype(jnp.bfloat16)
        returned = lax.all_to_all(results.reshape(ranks, capacity, width), "ep",
                                  split_axis=0, concat_axis=0, tiled=True)
        returned = returned.reshape(chunk, width)
        hit = token_pos[:, :, None] == slot_of[local][None, None, :]
        for part in (high, low):
            weight = jnp.sum(jnp.where(hit, part[:, :, None], 0.0), axis=1).astype(jnp.bfloat16)
            mixed = mixed + jnp.dot(weight, returned, preferred_element_type=jnp.float32)
    return (mixed.astype(jnp.bfloat16), backup)


def solution(mesh):
    torus = Mesh(mesh.devices.reshape(4, 4, mesh.shape["ep"]), ("grp_0", "grp_1", "ep"))
    tokens = P(GRP + ("ep",), None, None)
    pair_spec = P(GRP + ("ep",), None)
    state = P("ep", GRP, None)
    in_specs = (tokens, pair_spec, pair_spec, state, state, state, state)
    out_specs = (pair_spec, state)
    return jax.shard_map(body, mesh=torus, in_specs=in_specs, out_specs=out_specs, check_vma=False)
```

```python
import math

import jax
import jax.numpy as jnp
from jax import lax
from jax.sharding import Mesh
from jax.sharding import PartitionSpec as P

GRP = ("grp_0", "grp_1")

beta_one = 0.9
beta_two = 0.95
corr_one = 1.0 - 0.9**40
corr_two = 1.0 - 0.95**40
learn_rate = 0.05
decay_rate = 0.1
adam_eps = 1e-08
gate_unit = 65536.0


def adamw_step(master, moment_one, moment_two, gradient):
    widened = gradient.astype(jnp.float32)
    first_moment = beta_one * moment_one.astype(jnp.float32) + (1.0 - beta_one) * widened
    second_moment = beta_two * moment_two.astype(jnp.float32) + (1.0 - beta_two) * widened * widened
    return (
        first_moment / corr_one / (jnp.sqrt(second_moment / corr_two) + adam_eps)
        + decay_rate * master
    )


def slot_positions(ids, capacity):
    count = ids.shape[0]
    rows = lax.broadcasted_iota(jnp.int32, (count, count), 0)
    cols = lax.broadcasted_iota(jnp.int32, (count, count), 1)
    same = (ids[:, None] == ids[None, :]) & (cols < rows)
    slot_index = jnp.sum(same.astype(jnp.int32), axis=1)
    return ids * capacity + slot_index


def body(slot_hidden, expert_ids, gate_fixed, master, moment_one, moment_two, gradient):
    outer = lax.axis_size("grp_0")
    ranks = lax.axis_size("ep")
    local_experts = master.shape[0]
    experts = local_experts * ranks
    tok_count, top_count, hidden_width = slot_hidden.shape
    width = master.shape[2]
    capacity = max(2, tok_count * top_count // experts + tok_count * top_count // (2 * experts))
    slots = experts * capacity
    scaling = 1.0 / math.sqrt(hidden_width)

    step_dir = adamw_step(master, moment_one, moment_two, gradient)
    updated = master - learn_rate * step_dir
    weights = updated.astype(jnp.bfloat16)
    nearer = lax.all_gather(weights, "grp_1", axis=1, tiled=True)

    shift = outer // 2
    backup = lax.ppermute(step_dir, "grp_0", [(s, (s + shift) % outer) for s in range(outer)])

    pairs = tok_count * top_count
    positions = slot_positions(expert_ids.reshape(pairs), capacity)
    hidden_rows = slot_hidden.reshape(pairs, hidden_width)
    token_pos = positions.reshape(tok_count, top_count)
    high = (gate_fixed // 256).astype(jnp.float32) / 256.0
    low = (gate_fixed % 256).astype(jnp.float32) / gate_unit
    chunk = ranks * capacity

    column = lax.broadcasted_iota(jnp.int32, (chunk,), 0)
    slot_of = []
    arrived = []
    for local in range(local_experts):
        slot_of.append(((column // capacity) * local_experts + local) * capacity + column % capacity)
        placing = (positions[None, :] == slot_of[local][:, None]).astype(jnp.bfloat16)
        outgoing = jnp.dot(placing, hidden_rows, preferred_element_type=jnp.float32).astype(jnp.bfloat16)
        if local == 0:
            outgoing, nearer = lax.optimization_barrier((outgoing, nearer))
        arrived.append(lax.all_to_all(outgoing.reshape(ranks, capacity, hidden_width), "ep",
                                      split_axis=0, concat_axis=0, tiled=True))

    gathered = []
    for local in range(local_experts):
        rows = nearer[local]
        if gathered:
            rows, _ = lax.optimization_barrier((rows, gathered[-1]))
        gathered.append(lax.all_gather(rows, "grp_0", axis=0, tiled=True))

    mixed = jnp.zeros((tok_count, width), jnp.float32)
    for local in range(local_experts):
        product = jnp.dot(arrived[local].reshape(chunk, hidden_width), gathered[local],
                          preferred_element_type=jnp.float32)
        results = (product * scaling).astype(jnp.bfloat16)
        returned = lax.all_to_all(results.reshape(ranks, capacity, width), "ep",
                                  split_axis=0, concat_axis=0, tiled=True)
        returned = returned.reshape(chunk, width)
        hit = token_pos[:, :, None] == slot_of[local][None, None, :]
        for part in (high, low):
            weight = jnp.sum(jnp.where(hit, part[:, :, None], 0.0), axis=1).astype(jnp.bfloat16)
            mixed = mixed + jnp.dot(weight, returned, preferred_element_type=jnp.float32)
    return (mixed.astype(jnp.bfloat16), backup)


def solution(mesh):
    torus = Mesh(mesh.devices.reshape(4, 4, mesh.shape["ep"]), ("grp_0", "grp_1", "ep"))
    tokens = P(GRP + ("ep",), None, None)
    pair_spec = P(GRP + ("ep",), None)
    state = P("ep", GRP, None)
    in_specs = (tokens, pair_spec, pair_spec, state, state, state, state)
    out_specs = (pair_spec, state)
    return jax.shard_map(body, mesh=torus, in_specs=in_specs, out_specs=out_specs, check_vma=False)
```

```python
import math

import jax
import jax.numpy as jnp
from jax import lax
from jax.sharding import Mesh
from jax.sharding import PartitionSpec as P

GRP = ("grp_0", "grp_1")

beta_one = 0.9
beta_two = 0.95
corr_one = 1.0 - 0.9**40
corr_two = 1.0 - 0.95**40
learn_rate = 0.05
decay_rate = 0.1
adam_eps = 1e-08
gate_unit = 65536.0


def adamw_step(master, moment_one, moment_two, gradient):
    widened = gradient.astype(jnp.float32)
    first_moment = beta_one * moment_one.astype(jnp.float32) + (1.0 - beta_one) * widened
    second_moment = beta_two * moment_two.astype(jnp.float32) + (1.0 - beta_two) * widened * widened
    return (
        first_moment / corr_one / (jnp.sqrt(second_moment / corr_two) + adam_eps)
        + decay_rate * master
    )


def slot_positions(ids, capacity):
    count = ids.shape[0]
    rows = lax.broadcasted_iota(jnp.int32, (count, count), 0)
    cols = lax.broadcasted_iota(jnp.int32, (count, count), 1)
    same = (ids[:, None] == ids[None, :]) & (cols < rows)
    slot_index = jnp.sum(same.astype(jnp.int32), axis=1)
    return ids * capacity + slot_index


def body(slot_hidden, expert_ids, gate_fixed, master, moment_one, moment_two, gradient):
    outer = lax.axis_size("grp_0")
    ranks = lax.axis_size("ep")
    local_experts = master.shape[0]
    experts = local_experts * ranks
    tok_count, top_count, hidden_width = slot_hidden.shape
    width = master.shape[2]
    capacity = max(2, tok_count * top_count // experts + tok_count * top_count // (2 * experts))
    slots = experts * capacity
    scaling = 1.0 / math.sqrt(hidden_width)

    step_dir = adamw_step(master, moment_one, moment_two, gradient)
    updated = master - learn_rate * step_dir
    weights = updated.astype(jnp.bfloat16)
    nearer = lax.all_gather(weights, "grp_1", axis=1, tiled=True)

    shift = outer // 2
    backup = lax.ppermute(step_dir, "grp_0", [(s, (s + shift) % outer) for s in range(outer)])

    pairs = tok_count * top_count
    positions = slot_positions(expert_ids.reshape(pairs), capacity)
    hidden_rows = slot_hidden.reshape(pairs, hidden_width)
    token_pos = positions.reshape(tok_count, top_count)
    high = (gate_fixed // 256).astype(jnp.float32) / 256.0
    low = (gate_fixed % 256).astype(jnp.float32) / gate_unit
    chunk = ranks * capacity

    column = lax.broadcasted_iota(jnp.int32, (chunk,), 0)
    slot_of = []
    for local in range(local_experts):
        slot_of.append(((column // capacity) * local_experts + local) * capacity + column % capacity)
    every_slot = lax.broadcasted_iota(jnp.int32, (slots,), 0)
    placing = (positions[None, :] == every_slot[:, None]).astype(jnp.bfloat16)
    outgoing = jnp.dot(placing, hidden_rows, preferred_element_type=jnp.float32).astype(jnp.bfloat16)
    delivered = lax.all_to_all(outgoing.reshape(ranks, local_experts * capacity, hidden_width), "ep",
                               split_axis=0, concat_axis=0, tiled=True)
    delivered = delivered.reshape(ranks, local_experts, capacity, hidden_width)
    arrived = [delivered[:, local] for local in range(local_experts)]

    gathered = []
    for local in range(local_experts):
        rows, tie = lax.optimization_barrier((nearer[local], gathered[-1] if gathered else arrived[0]))
        if not gathered:
            arrived[0] = tie
        gathered.append(lax.all_gather(rows, "grp_0", axis=0, tiled=True))

    mixed = jnp.zeros((tok_count, width), jnp.float32)
    for local in range(local_experts):
        product = jnp.dot(arrived[local].reshape(chunk, hidden_width), gathered[local],
                          preferred_element_type=jnp.float32)
        results = (product * scaling).astype(jnp.bfloat16)
        returned = lax.all_to_all(results.reshape(ranks, capacity, width), "ep",
                                  split_axis=0, concat_axis=0, tiled=True)
        returned = returned.reshape(chunk, width)
        hit = token_pos[:, :, None] == slot_of[local][None, None, :]
        for part in (high, low):
            weight = jnp.sum(jnp.where(hit, part[:, :, None], 0.0), axis=1).astype(jnp.bfloat16)
            mixed = mixed + jnp.dot(weight, returned, preferred_element_type=jnp.float32)
    return (mixed.astype(jnp.bfloat16), backup)


def solution(mesh):
    torus = Mesh(mesh.devices.reshape(4, 4, mesh.shape["ep"]), ("grp_0", "grp_1", "ep"))
    tokens = P(GRP + ("ep",), None, None)
    pair_spec = P(GRP + ("ep",), None)
    state = P("ep", GRP, None)
    in_specs = (tokens, pair_spec, pair_spec, state, state, state, state)
    out_specs = (pair_spec, state)
    return jax.shard_map(body, mesh=torus, in_specs=in_specs, out_specs=out_specs, check_vma=False)
```

```python
import math

import jax
import jax.numpy as jnp
from jax import lax
from jax.sharding import Mesh
from jax.sharding import PartitionSpec as P

GRP = ("grp_0", "grp_1")

beta_one = 0.9
beta_two = 0.95
corr_one = 1.0 - 0.9**40
corr_two = 1.0 - 0.95**40
learn_rate = 0.05
decay_rate = 0.1
adam_eps = 1e-08
gate_unit = 65536.0


def adamw_step(master, moment_one, moment_two, gradient):
    widened = gradient.astype(jnp.float32)
    first_moment = beta_one * moment_one.astype(jnp.float32) + (1.0 - beta_one) * widened
    second_moment = beta_two * moment_two.astype(jnp.float32) + (1.0 - beta_two) * widened * widened
    return (
        first_moment / corr_one / (jnp.sqrt(second_moment / corr_two) + adam_eps)
        + decay_rate * master
    )


def slot_positions(ids, capacity):
    count = ids.shape[0]
    rows = lax.broadcasted_iota(jnp.int32, (count, count), 0)
    cols = lax.broadcasted_iota(jnp.int32, (count, count), 1)
    same = (ids[:, None] == ids[None, :]) & (cols < rows)
    slot_index = jnp.sum(same.astype(jnp.int32), axis=1)
    return ids * capacity + slot_index


def body(slot_hidden, expert_ids, gate_fixed, master, moment_one, moment_two, gradient):
    outer = lax.axis_size("grp_0")
    ranks = lax.axis_size("ep")
    local_experts = master.shape[0]
    experts = local_experts * ranks
    tok_count, top_count, hidden_width = slot_hidden.shape
    width = master.shape[2]
    capacity = max(2, tok_count * top_count // experts + tok_count * top_count // (2 * experts))
    slots = experts * capacity
    scaling = 1.0 / math.sqrt(hidden_width)

    step_dir = adamw_step(master, moment_one, moment_two, gradient)
    updated = master - learn_rate * step_dir
    weights = updated.astype(jnp.bfloat16)

    shift = outer // 2
    backup = lax.ppermute(step_dir, "grp_0", [(s, (s + shift) % outer) for s in range(outer)])

    pairs = tok_count * top_count
    positions = slot_positions(expert_ids.reshape(pairs), capacity)
    hidden_rows = slot_hidden.reshape(pairs, hidden_width)
    token_pos = positions.reshape(tok_count, top_count)
    high = (gate_fixed // 256).astype(jnp.float32) / 256.0
    low = (gate_fixed % 256).astype(jnp.float32) / gate_unit
    chunk = ranks * capacity

    column = lax.broadcasted_iota(jnp.int32, (chunk,), 0)
    slot_of = []
    arrived = []
    for local in range(local_experts):
        slot_of.append(((column // capacity) * local_experts + local) * capacity + column % capacity)
        placing = (positions[None, :] == slot_of[local][:, None]).astype(jnp.bfloat16)
        outgoing = jnp.dot(placing, hidden_rows, preferred_element_type=jnp.float32).astype(jnp.bfloat16)
        arrived.append(lax.all_to_all(outgoing.reshape(ranks, capacity, hidden_width), "ep",
                                      split_axis=0, concat_axis=0, tiled=True))

    gathered = []
    for local in range(local_experts):
        own = weights[local]
        if gathered:
            own, _ = lax.optimization_barrier((own, gathered[-1]))
        rows = lax.all_gather(own, "grp_1", axis=0, tiled=True)
        rows, tie = lax.optimization_barrier((rows, gathered[-1] if gathered else arrived[0]))
        if not gathered:
            arrived[0] = tie
        gathered.append(lax.all_gather(rows, "grp_0", axis=0, tiled=True))

    mixed = jnp.zeros((tok_count, width), jnp.float32)
    for local in range(local_experts):
        product = jnp.dot(arrived[local].reshape(chunk, hidden_width), gathered[local],
                          preferred_element_type=jnp.float32)
        results = (product * scaling).astype(jnp.bfloat16)
        returned = lax.all_to_all(results.reshape(ranks, capacity, width), "ep",
                                  split_axis=0, concat_axis=0, tiled=True)
        returned = returned.reshape(chunk, width)
        hit = token_pos[:, :, None] == slot_of[local][None, None, :]
        for part in (high, low):
            weight = jnp.sum(jnp.where(hit, part[:, :, None], 0.0), axis=1).astype(jnp.bfloat16)
            mixed = mixed + jnp.dot(weight, returned, preferred_element_type=jnp.float32)
    return (mixed.astype(jnp.bfloat16), backup)


def solution(mesh):
    torus = Mesh(mesh.devices.reshape(4, 4, mesh.shape["ep"]), ("grp_0", "grp_1", "ep"))
    tokens = P(GRP + ("ep",), None, None)
    pair_spec = P(GRP + ("ep",), None)
    state = P("ep", GRP, None)
    in_specs = (tokens, pair_spec, pair_spec, state, state, state, state)
    out_specs = (pair_spec, state)
    return jax.shard_map(body, mesh=torus, in_specs=in_specs, out_specs=out_specs, check_vma=False)
```

```python
import math

import jax
import jax.numpy as jnp
from jax import lax
from jax.sharding import Mesh
from jax.sharding import PartitionSpec as P

GRP = ("grp_0", "grp_1")

beta_one = 0.9
beta_two = 0.95
corr_one = 1.0 - 0.9**40
corr_two = 1.0 - 0.95**40
learn_rate = 0.05
decay_rate = 0.1
adam_eps = 1e-08
gate_unit = 65536.0


def adamw_step(master, moment_one, moment_two, gradient):
    widened = gradient.astype(jnp.float32)
    first_moment = beta_one * moment_one.astype(jnp.float32) + (1.0 - beta_one) * widened
    second_moment = beta_two * moment_two.astype(jnp.float32) + (1.0 - beta_two) * widened * widened
    return (
        first_moment / corr_one / (jnp.sqrt(second_moment / corr_two) + adam_eps)
        + decay_rate * master
    )


def slot_positions(ids, capacity):
    count = ids.shape[0]
    rows = lax.broadcasted_iota(jnp.int32, (count, count), 0)
    cols = lax.broadcasted_iota(jnp.int32, (count, count), 1)
    same = (ids[:, None] == ids[None, :]) & (cols < rows)
    slot_index = jnp.sum(same.astype(jnp.int32), axis=1)
    return ids * capacity + slot_index


def body(slot_hidden, expert_ids, gate_fixed, master, moment_one, moment_two, gradient):
    outer = lax.axis_size("grp_0")
    ranks = lax.axis_size("ep")
    local_experts = master.shape[0]
    experts = local_experts * ranks
    tok_count, top_count, hidden_width = slot_hidden.shape
    width = master.shape[2]
    capacity = max(2, tok_count * top_count // experts + tok_count * top_count // (2 * experts))
    slots = experts * capacity
    scaling = 1.0 / math.sqrt(hidden_width)

    step_dir = adamw_step(master, moment_one, moment_two, gradient)
    updated = master - learn_rate * step_dir
    weights = updated.astype(jnp.bfloat16)

    shift = outer // 2
    backup = lax.ppermute(step_dir, "grp_0", [(s, (s + shift) % outer) for s in range(outer)])

    pairs = tok_count * top_count
    positions = slot_positions(expert_ids.reshape(pairs), capacity)
    hidden_rows = slot_hidden.reshape(pairs, hidden_width)
    token_pos = positions.reshape(tok_count, top_count)
    high = (gate_fixed // 256).astype(jnp.float32) / 256.0
    low = (gate_fixed % 256).astype(jnp.float32) / gate_unit
    chunk = ranks * capacity

    column = lax.broadcasted_iota(jnp.int32, (chunk,), 0)
    slot_of = []
    arrived = []
    for local in range(local_experts):
        slot_of.append(((column // capacity) * local_experts + local) * capacity + column % capacity)
        placing = (positions[None, :] == slot_of[local][:, None]).astype(jnp.bfloat16)
        outgoing = jnp.dot(placing, hidden_rows, preferred_element_type=jnp.float32).astype(jnp.bfloat16)
        arrived.append(lax.all_to_all(outgoing.reshape(ranks, capacity, hidden_width), "ep",
                                      split_axis=0, concat_axis=0, tiled=True))

    gathered = []
    first_stage = []
    for local in range(local_experts):
        own = weights[local]
        if first_stage:
            own, _ = lax.optimization_barrier((own, arrived[0]))
        rows = lax.all_gather(own, "grp_1", axis=0, tiled=True)
        first_stage.append(rows)
        rows, tie = lax.optimization_barrier((rows, gathered[-1] if gathered else arrived[0]))
        if not gathered:
            arrived[0] = tie
        gathered.append(lax.all_gather(rows, "grp_0", axis=0, tiled=True))

    mixed = jnp.zeros((tok_count, width), jnp.float32)
    for local in range(local_experts):
        product = jnp.dot(arrived[local].reshape(chunk, hidden_width), gathered[local],
                          preferred_element_type=jnp.float32)
        results = (product * scaling).astype(jnp.bfloat16)
        if local + 1 < local_experts:
            results, _ = lax.optimization_barrier((results, first_stage[local + 1]))
        returned = lax.all_to_all(results.reshape(ranks, capacity, width), "ep",
                                  split_axis=0, concat_axis=0, tiled=True)
        returned = returned.reshape(chunk, width)
        hit = token_pos[:, :, None] == slot_of[local][None, None, :]
        for part in (high, low):
            weight = jnp.sum(jnp.where(hit, part[:, :, None], 0.0), axis=1).astype(jnp.bfloat16)
            mixed = mixed + jnp.dot(weight, returned, preferred_element_type=jnp.float32)
    return (mixed.astype(jnp.bfloat16), backup)


def solution(mesh):
    torus = Mesh(mesh.devices.reshape(4, 4, mesh.shape["ep"]), ("grp_0", "grp_1", "ep"))
    tokens = P(GRP + ("ep",), None, None)
    pair_spec = P(GRP + ("ep",), None)
    state = P("ep", GRP, None)
    in_specs = (tokens, pair_spec, pair_spec, state, state, state, state)
    out_specs = (pair_spec, state)
    return jax.shard_map(body, mesh=torus, in_specs=in_specs, out_specs=out_specs, check_vma=False)
```

```python
import math

import jax
import jax.numpy as jnp
from jax import lax
from jax.sharding import Mesh
from jax.sharding import PartitionSpec as P

GRP = ("grp_0", "grp_1")

beta_one = 0.9
beta_two = 0.95
corr_one = 1.0 - 0.9**40
corr_two = 1.0 - 0.95**40
learn_rate = 0.05
decay_rate = 0.1
adam_eps = 1e-08
gate_unit = 65536.0


def adamw_step(master, moment_one, moment_two, gradient):
    widened = gradient.astype(jnp.float32)
    first_moment = beta_one * moment_one.astype(jnp.float32) + (1.0 - beta_one) * widened
    second_moment = beta_two * moment_two.astype(jnp.float32) + (1.0 - beta_two) * widened * widened
    return (
        first_moment / corr_one / (jnp.sqrt(second_moment / corr_two) + adam_eps)
        + decay_rate * master
    )


def slot_positions(ids, capacity):
    count = ids.shape[0]
    rows = lax.broadcasted_iota(jnp.int32, (count, count), 0)
    cols = lax.broadcasted_iota(jnp.int32, (count, count), 1)
    same = (ids[:, None] == ids[None, :]) & (cols < rows)
    slot_index = jnp.sum(same.astype(jnp.int32), axis=1)
    return ids * capacity + slot_index


def body(slot_hidden, expert_ids, gate_fixed, master, moment_one, moment_two, gradient):
    outer = lax.axis_size("grp_0")
    ranks = lax.axis_size("ep")
    local_experts = master.shape[0]
    experts = local_experts * ranks
    tok_count, top_count, hidden_width = slot_hidden.shape
    width = master.shape[2]
    capacity = max(2, tok_count * top_count // experts + tok_count * top_count // (2 * experts))
    slots = experts * capacity
    scaling = 1.0 / math.sqrt(hidden_width)

    step_dir = adamw_step(master, moment_one, moment_two, gradient)
    updated = master - learn_rate * step_dir
    weights = updated.astype(jnp.bfloat16)

    shift = outer // 2
    backup = lax.ppermute(step_dir, "grp_0", [(s, (s + shift) % outer) for s in range(outer)])

    pairs = tok_count * top_count
    positions = slot_positions(expert_ids.reshape(pairs), capacity)
    hidden_rows = slot_hidden.reshape(pairs, hidden_width)
    token_pos = positions.reshape(tok_count, top_count)
    high = (gate_fixed // 256).astype(jnp.float32) / 256.0
    low = (gate_fixed % 256).astype(jnp.float32) / gate_unit
    chunk = ranks * capacity

    column = lax.broadcasted_iota(jnp.int32, (chunk,), 0)
    slot_of = []
    arrived = []
    for local in range(local_experts):
        slot_of.append(((column // capacity) * local_experts + local) * capacity + column % capacity)
        placing = (positions[None, :] == slot_of[local][:, None]).astype(jnp.bfloat16)
        outgoing = jnp.dot(placing, hidden_rows, preferred_element_type=jnp.float32).astype(jnp.bfloat16)
        arrived.append(lax.all_to_all(outgoing.reshape(ranks, capacity, hidden_width), "ep",
                                      split_axis=0, concat_axis=0, tiled=True))

    inner = lax.axis_size("grp_1")
    here = lax.axis_index("grp_1")
    gathered = []
    first_stage = []
    for local in range(local_experts):
        own = weights[local]
        if first_stage:
            own, _ = lax.optimization_barrier((own, arrived[0]))
        if first_stage:
            rows = lax.all_gather(own, "grp_1", axis=0, tiled=True)
        else:
            received = [own] + [lax.ppermute(own, "grp_1", [(s, (s + k) % inner) for s in range(inner)])
                                for k in range(1, inner)]
            ordered = jnp.stack([received[(-k) % inner] for k in range(inner)], axis=0)
            rows = jnp.roll(ordered, here, axis=0).reshape(inner * own.shape[0], width)
        first_stage.append(rows)
        rows, tie = lax.optimization_barrier((rows, gathered[-1] if gathered else arrived[0]))
        if not gathered:
            arrived[0] = tie
        gathered.append(lax.all_gather(rows, "grp_0", axis=0, tiled=True))

    mixed = jnp.zeros((tok_count, width), jnp.float32)
    for local in range(local_experts):
        product = jnp.dot(arrived[local].reshape(chunk, hidden_width), gathered[local],
                          preferred_element_type=jnp.float32)
        results = (product * scaling).astype(jnp.bfloat16)
        if local + 1 < local_experts:
            results, _ = lax.optimization_barrier((results, first_stage[local + 1]))
        returned = lax.all_to_all(results.reshape(ranks, capacity, width), "ep",
                                  split_axis=0, concat_axis=0, tiled=True)
        returned = returned.reshape(chunk, width)
        hit = token_pos[:, :, None] == slot_of[local][None, None, :]
        for part in (high, low):
            weight = jnp.sum(jnp.where(hit, part[:, :, None], 0.0), axis=1).astype(jnp.bfloat16)
            mixed = mixed + jnp.dot(weight, returned, preferred_element_type=jnp.float32)
    return (mixed.astype(jnp.bfloat16), backup)


def solution(mesh):
    torus = Mesh(mesh.devices.reshape(4, 4, mesh.shape["ep"]), ("grp_0", "grp_1", "ep"))
    tokens = P(GRP + ("ep",), None, None)
    pair_spec = P(GRP + ("ep",), None)
    state = P("ep", GRP, None)
    in_specs = (tokens, pair_spec, pair_spec, state, state, state, state)
    out_specs = (pair_spec, state)
    return jax.shard_map(body, mesh=torus, in_specs=in_specs, out_specs=out_specs, check_vma=False)
```

```python
import math

import jax
import jax.numpy as jnp
from jax import lax
from jax.sharding import Mesh
from jax.sharding import PartitionSpec as P

GRP = ("grp_0", "grp_1")

beta_one = 0.9
beta_two = 0.95
corr_one = 1.0 - 0.9**40
corr_two = 1.0 - 0.95**40
learn_rate = 0.05
decay_rate = 0.1
adam_eps = 1e-08
gate_unit = 65536.0


def adamw_step(master, moment_one, moment_two, gradient):
    widened = gradient.astype(jnp.float32)
    first_moment = beta_one * moment_one.astype(jnp.float32) + (1.0 - beta_one) * widened
    second_moment = beta_two * moment_two.astype(jnp.float32) + (1.0 - beta_two) * widened * widened
    return (
        first_moment / corr_one / (jnp.sqrt(second_moment / corr_two) + adam_eps)
        + decay_rate * master
    )


def slot_positions(ids, capacity):
    count = ids.shape[0]
    rows = lax.broadcasted_iota(jnp.int32, (count, count), 0)
    cols = lax.broadcasted_iota(jnp.int32, (count, count), 1)
    same = (ids[:, None] == ids[None, :]) & (cols < rows)
    slot_index = jnp.sum(same.astype(jnp.int32), axis=1)
    return ids * capacity + slot_index


def body(slot_hidden, expert_ids, gate_fixed, master, moment_one, moment_two, gradient):
    outer = lax.axis_size("grp_0")
    ranks = lax.axis_size("ep")
    local_experts = master.shape[0]
    experts = local_experts * ranks
    tok_count, top_count, hidden_width = slot_hidden.shape
    width = master.shape[2]
    capacity = max(2, tok_count * top_count // experts + tok_count * top_count // (2 * experts))
    slots = experts * capacity
    scaling = 1.0 / math.sqrt(hidden_width)

    step_dir = adamw_step(master, moment_one, moment_two, gradient)
    updated = master - learn_rate * step_dir
    weights = updated.astype(jnp.bfloat16)

    shift = outer // 2
    backup = lax.ppermute(step_dir, "grp_0", [(s, (s + shift) % outer) for s in range(outer)])

    pairs = tok_count * top_count
    positions = slot_positions(expert_ids.reshape(pairs), capacity)
    hidden_rows = slot_hidden.reshape(pairs, hidden_width)
    token_pos = positions.reshape(tok_count, top_count)
    high = (gate_fixed // 256).astype(jnp.float32) / 256.0
    low = (gate_fixed % 256).astype(jnp.float32) / gate_unit
    chunk = ranks * capacity

    column = lax.broadcasted_iota(jnp.int32, (chunk,), 0)
    slot_of = []
    arrived = []
    for local in range(local_experts):
        slot_of.append(((column // capacity) * local_experts + local) * capacity + column % capacity)
        placing = (positions[None, :] == slot_of[local][:, None]).astype(jnp.bfloat16)
        outgoing = jnp.dot(placing, hidden_rows, preferred_element_type=jnp.float32).astype(jnp.bfloat16)
        arrived.append(lax.all_to_all(outgoing.reshape(ranks, capacity, hidden_width), "ep",
                                      split_axis=0, concat_axis=0, tiled=True))

    inner = lax.axis_size("grp_1")
    here = lax.axis_index("grp_1")
    gathered = []
    first_stage = []
    for local in range(local_experts):
        own = weights[local]
        if first_stage:
            own, _ = lax.optimization_barrier((own, arrived[0]))
        if first_stage:
            rows = lax.all_gather(own, "grp_1", axis=0, tiled=True)
        else:
            received = [own] + [lax.ppermute(own, "grp_1", [(s, (s + k) % inner) for s in range(inner)])
                                for k in range(1, inner)]
            ordered = jnp.stack([received[(-k) % inner] for k in range(inner)], axis=0)
            rows = jnp.roll(ordered, here, axis=0).reshape(inner * own.shape[0], width)
        first_stage.append(rows)
        if gathered:
            rows, _ = lax.optimization_barrier((rows, gathered[-1]))
        gathered.append(lax.all_gather(rows, "grp_0", axis=0, tiled=True))

    mixed = jnp.zeros((tok_count, width), jnp.float32)
    for local in range(local_experts):
        product = jnp.dot(arrived[local].reshape(chunk, hidden_width), gathered[local],
                          preferred_element_type=jnp.float32)
        results = (product * scaling).astype(jnp.bfloat16)
        if local + 1 < local_experts:
            results, _ = lax.optimization_barrier((results, first_stage[local + 1]))
        returned = lax.all_to_all(results.reshape(ranks, capacity, width), "ep",
                                  split_axis=0, concat_axis=0, tiled=True)
        returned = returned.reshape(chunk, width)
        hit = token_pos[:, :, None] == slot_of[local][None, None, :]
        for part in (high, low):
            weight = jnp.sum(jnp.where(hit, part[:, :, None], 0.0), axis=1).astype(jnp.bfloat16)
            mixed = mixed + jnp.dot(weight, returned, preferred_element_type=jnp.float32)
    return (mixed.astype(jnp.bfloat16), backup)


def solution(mesh):
    torus = Mesh(mesh.devices.reshape(4, 4, mesh.shape["ep"]), ("grp_0", "grp_1", "ep"))
    tokens = P(GRP + ("ep",), None, None)
    pair_spec = P(GRP + ("ep",), None)
    state = P("ep", GRP, None)
    in_specs = (tokens, pair_spec, pair_spec, state, state, state, state)
    out_specs = (pair_spec, state)
    return jax.shard_map(body, mesh=torus, in_specs=in_specs, out_specs=out_specs, check_vma=False)
```

```python
import math

import jax
import jax.numpy as jnp
from jax import lax
from jax.sharding import Mesh
from jax.sharding import PartitionSpec as P

GRP = ("grp_0", "grp_1")

beta_one = 0.9
beta_two = 0.95
corr_one = 1.0 - 0.9**40
corr_two = 1.0 - 0.95**40
learn_rate = 0.05
decay_rate = 0.1
adam_eps = 1e-08
gate_unit = 65536.0


def adamw_step(master, moment_one, moment_two, gradient):
    widened = gradient.astype(jnp.float32)
    first_moment = beta_one * moment_one.astype(jnp.float32) + (1.0 - beta_one) * widened
    second_moment = beta_two * moment_two.astype(jnp.float32) + (1.0 - beta_two) * widened * widened
    return (
        first_moment / corr_one / (jnp.sqrt(second_moment / corr_two) + adam_eps)
        + decay_rate * master
    )


def slot_positions(ids, capacity):
    count = ids.shape[0]
    rows = lax.broadcasted_iota(jnp.int32, (count, count), 0)
    cols = lax.broadcasted_iota(jnp.int32, (count, count), 1)
    same = (ids[:, None] == ids[None, :]) & (cols < rows)
    slot_index = jnp.sum(same.astype(jnp.int32), axis=1)
    return ids * capacity + slot_index


def body(slot_hidden, expert_ids, gate_fixed, master, moment_one, moment_two, gradient):
    outer = lax.axis_size("grp_0")
    ranks = lax.axis_size("ep")
    local_experts = master.shape[0]
    experts = local_experts * ranks
    tok_count, top_count, hidden_width = slot_hidden.shape
    width = master.shape[2]
    capacity = max(2, tok_count * top_count // experts + tok_count * top_count // (2 * experts))
    slots = experts * capacity
    scaling = 1.0 / math.sqrt(hidden_width)

    step_dir = adamw_step(master, moment_one, moment_two, gradient)
    updated = master - learn_rate * step_dir
    weights = updated.astype(jnp.bfloat16)

    shift = outer // 2
    backup = lax.ppermute(step_dir, "grp_0", [(s, (s + shift) % outer) for s in range(outer)])

    pairs = tok_count * top_count
    positions = slot_positions(expert_ids.reshape(pairs), capacity)
    hidden_rows = slot_hidden.reshape(pairs, hidden_width)
    token_pos = positions.reshape(tok_count, top_count)
    high = (gate_fixed // 256).astype(jnp.float32) / 256.0
    low = (gate_fixed % 256).astype(jnp.float32) / gate_unit
    chunk = ranks * capacity

    column = lax.broadcasted_iota(jnp.int32, (chunk,), 0)
    slot_of = []
    arrived = []
    for local in range(local_experts):
        slot_of.append(((column // capacity) * local_experts + local) * capacity + column % capacity)
        placing = (positions[None, :] == slot_of[local][:, None]).astype(jnp.bfloat16)
        outgoing = jnp.dot(placing, hidden_rows, preferred_element_type=jnp.float32).astype(jnp.bfloat16)
        arrived.append(lax.all_to_all(outgoing.reshape(ranks, capacity, hidden_width), "ep",
                                      split_axis=0, concat_axis=0, tiled=True))

    inner = lax.axis_size("grp_1")
    here = lax.axis_index("grp_1")
    gathered = []
    first_stage = []
    for local in range(local_experts):
        own = weights[local]
        if first_stage:
            own, _ = lax.optimization_barrier((own, arrived[0]))
        if first_stage:
            received = [own] + [lax.ppermute(own, "grp_1", [(s, (s + k) % inner) for s in range(inner)])
                                for k in range(1, inner)]
            ordered = jnp.stack([received[(-k) % inner] for k in range(inner)], axis=0)
            rows = jnp.roll(ordered, here, axis=0).reshape(inner * own.shape[0], width)
        else:
            rows = lax.all_gather(own, "grp_1", axis=0, tiled=True)
        first_stage.append(rows)
        rows, tie = lax.optimization_barrier((rows, gathered[-1] if gathered else arrived[0]))
        if not gathered:
            arrived[0] = tie
        gathered.append(lax.all_gather(rows, "grp_0", axis=0, tiled=True))

    mixed = jnp.zeros((tok_count, width), jnp.float32)
    for local in range(local_experts):
        product = jnp.dot(arrived[local].reshape(chunk, hidden_width), gathered[local],
                          preferred_element_type=jnp.float32)
        results = (product * scaling).astype(jnp.bfloat16)
        if local + 1 < local_experts:
            results, _ = lax.optimization_barrier((results, first_stage[local + 1]))
        returned = lax.all_to_all(results.reshape(ranks, capacity, width), "ep",
                                  split_axis=0, concat_axis=0, tiled=True)
        returned = returned.reshape(chunk, width)
        hit = token_pos[:, :, None] == slot_of[local][None, None, :]
        for part in (high, low):
            weight = jnp.sum(jnp.where(hit, part[:, :, None], 0.0), axis=1).astype(jnp.bfloat16)
            mixed = mixed + jnp.dot(weight, returned, preferred_element_type=jnp.float32)
    return (mixed.astype(jnp.bfloat16), backup)


def solution(mesh):
    torus = Mesh(mesh.devices.reshape(4, 4, mesh.shape["ep"]), ("grp_0", "grp_1", "ep"))
    tokens = P(GRP + ("ep",), None, None)
    pair_spec = P(GRP + ("ep",), None)
    state = P("ep", GRP, None)
    in_specs = (tokens, pair_spec, pair_spec, state, state, state, state)
    out_specs = (pair_spec, state)
    return jax.shard_map(body, mesh=torus, in_specs=in_specs, out_specs=out_specs, check_vma=False)
```

```python
import math

import jax
import jax.numpy as jnp
from jax import lax
from jax.sharding import Mesh
from jax.sharding import PartitionSpec as P

GRP = ("grp_0", "grp_1")

beta_one = 0.9
beta_two = 0.95
corr_one = 1.0 - 0.9**40
corr_two = 1.0 - 0.95**40
learn_rate = 0.05
decay_rate = 0.1
adam_eps = 1e-08
gate_unit = 65536.0


def adamw_step(master, moment_one, moment_two, gradient):
    widened = gradient.astype(jnp.float32)
    first_moment = beta_one * moment_one.astype(jnp.float32) + (1.0 - beta_one) * widened
    second_moment = beta_two * moment_two.astype(jnp.float32) + (1.0 - beta_two) * widened * widened
    return (
        first_moment / corr_one / (jnp.sqrt(second_moment / corr_two) + adam_eps)
        + decay_rate * master
    )


def slot_positions(ids, capacity):
    count = ids.shape[0]
    rows = lax.broadcasted_iota(jnp.int32, (count, count), 0)
    cols = lax.broadcasted_iota(jnp.int32, (count, count), 1)
    same = (ids[:, None] == ids[None, :]) & (cols < rows)
    slot_index = jnp.sum(same.astype(jnp.int32), axis=1)
    return ids * capacity + slot_index


def body(slot_hidden, expert_ids, gate_fixed, master, moment_one, moment_two, gradient):
    outer = lax.axis_size("grp_0")
    ranks = lax.axis_size("ep")
    local_experts = master.shape[0]
    experts = local_experts * ranks
    tok_count, top_count, hidden_width = slot_hidden.shape
    width = master.shape[2]
    capacity = max(2, tok_count * top_count // experts + tok_count * top_count // (2 * experts))
    slots = experts * capacity
    scaling = 1.0 / math.sqrt(hidden_width)

    step_dir = adamw_step(master, moment_one, moment_two, gradient)
    updated = master - learn_rate * step_dir
    weights = updated.astype(jnp.bfloat16)

    shift = outer // 2
    backup = lax.ppermute(step_dir, "grp_0", [(s, (s + shift) % outer) for s in range(outer)])

    pairs = tok_count * top_count
    positions = slot_positions(expert_ids.reshape(pairs), capacity)
    hidden_rows = slot_hidden.reshape(pairs, hidden_width)
    token_pos = positions.reshape(tok_count, top_count)
    high = (gate_fixed // 256).astype(jnp.float32) / 256.0
    low = (gate_fixed % 256).astype(jnp.float32) / gate_unit
    chunk = ranks * capacity

    column = lax.broadcasted_iota(jnp.int32, (chunk,), 0)
    slot_of = []
    arrived = []
    for local in range(local_experts):
        slot_of.append(((column // capacity) * local_experts + local) * capacity + column % capacity)
        placing = (positions[None, :] == slot_of[local][:, None]).astype(jnp.bfloat16)
        outgoing = jnp.dot(placing, hidden_rows, preferred_element_type=jnp.float32).astype(jnp.bfloat16)
        arrived.append(lax.all_to_all(outgoing.reshape(ranks, capacity, hidden_width), "ep",
                                      split_axis=0, concat_axis=0, tiled=True))

    gathered = []
    first_stage = []
    for local in range(local_experts):
        own = weights[local]
        if first_stage:
            own, _ = lax.optimization_barrier((own, arrived[0]))
        rows = lax.all_gather(own, "grp_1", axis=0, tiled=True)
        first_stage.append(rows)
        rows, tie = lax.optimization_barrier((rows, gathered[-1] if gathered else arrived[0]))
        if not gathered:
            arrived[0] = tie
        gathered.append(lax.all_gather(rows, "grp_0", axis=0, tiled=True))

    mixed = jnp.zeros((tok_count, width), jnp.float32)
    for local in range(local_experts):
        product = jnp.dot(arrived[local].reshape(chunk, hidden_width), gathered[local],
                          preferred_element_type=jnp.float32)
        results = (product * scaling).astype(jnp.bfloat16)
        if local + 1 < local_experts:
            results, _ = lax.optimization_barrier((results, first_stage[local + 1]))
        returned = lax.all_to_all(results.reshape(ranks, capacity, width), "ep",
                                  split_axis=0, concat_axis=0, tiled=True)
        returned = returned.reshape(chunk, width)
        hit = token_pos[:, :, None] == slot_of[local][None, None, :]
        weight = jnp.concatenate(
            [jnp.sum(jnp.where(hit, part[:, :, None], 0.0), axis=1) for part in (high, low)], axis=0)
        both = jnp.dot(weight.astype(jnp.bfloat16), returned, preferred_element_type=jnp.float32)
        mixed = mixed + both[:tok_count] + both[tok_count:]
    return (mixed.astype(jnp.bfloat16), backup)


def solution(mesh):
    torus = Mesh(mesh.devices.reshape(4, 4, mesh.shape["ep"]), ("grp_0", "grp_1", "ep"))
    tokens = P(GRP + ("ep",), None, None)
    pair_spec = P(GRP + ("ep",), None)
    state = P("ep", GRP, None)
    in_specs = (tokens, pair_spec, pair_spec, state, state, state, state)
    out_specs = (pair_spec, state)
    return jax.shard_map(body, mesh=torus, in_specs=in_specs, out_specs=out_specs, check_vma=False)
```
